512 devices in a mesh: dp: 16 (over z, core), ctx: 32 (over y, x).
Axes of the slice: x: 4, y: 8, z: 8, core: 2. Of those that a mesh axis runs over, the one named last changes fastest.
Arguments:
- positions: int32 [49152], P('dp'), parts along dimension 0, may hold values from 0 to 24575, as said below
- queries: bfloat16 [147456, 2048], P(('dp', 'ctx')), parts along dimension 0, may hold values from -12 to 12
- keys_values: bfloat16 [147456, 1024], P(('dp', 'ctx')), parts along dimension 0, may hold values from -12 to 12
- router_weight: bfloat16 [147456], P(('dp', 'ctx')), parts along dimension 0, may hold values from 0.25 to 2
Outputs:
- attended: bfloat16 [147456, 2048], P(('dp', 'ctx')), parts along dimension 0
The draws below stay inside these ranges and needn't reach their ends.
There are 16 independent parts, one for each index of `dp`. The reference program is written for one: setup_inputs(seed, part) draws one part's arguments, and reference() takes and returns one part's arrays. A program takes and returns all parts, laid end to end along the dimension named above; each array names one. Nothing has to cross between parts.
Inputs may be any that keep to these rules, and one draw needn't show every extreme that they name: Distinct and increasing. The shard of positions d * 768 to (d + 1) * 768 - 1 holds at most 288 of them, and one shard holds exactly 288; slots of device d's blocks beyond counts[d] hold data that no output reads.
All inputs are finite; a program needn't handle non-finite values.
Results may differ from the reference program's by a relative error of at most 0.0085.
Values may be sent and summed in bfloat16 or wider, within the bound.
No kernel may reach another device: no remote copies, remote signals or barrier semaphores. Data moves between devices by JAX's collectives and lax.ppermute only.
A program may use at most 64 MiB of HBM per device.

```python
import math
import jax
import jax.numpy as jnp
from jax import lax

QUERY_HEADS = 16
KEY_VALUE_HEADS = 4
HEAD_SIZE = 128
TOK_DEV = 768
CAP = 288
SELECTED_TOKENS = 3072
N_CTX = 32


def selection_counts(key):
    key_pair = jax.random.split(jax.random.fold_in(key, 5), 2)
    busiest = jax.random.randint(key_pair[0], (), 0, N_CTX)
    shares = jax.random.randint(key_pair[1], (N_CTX,), 1, 4)
    shard_ids = jnp.arange(N_CTX, dtype=jnp.int32)
    others = shard_ids != busiest
    shares = jnp.where(others, shares, 0)
    remaining = SELECTED_TOKENS - CAP
    base_counts = remaining * shares // jnp.sum(shares)
    leftover = remaining - jnp.sum(base_counts)
    order_ids = jnp.cumsum(others.astype(jnp.int32)) - 1
    extra = (others & (order_ids < leftover)).astype(jnp.int32)
    return jnp.where(others, base_counts + extra, CAP).astype(jnp.int32)


def draw_positions(key, part):
    counts = selection_counts(key)
    shard_keys = jax.random.split(jax.random.fold_in(key, 7), N_CTX)

    def shard_mask(shard_key, shard_count):
        shuffled = jax.random.permutation(shard_key, TOK_DEV)
        chosen = (jnp.arange(TOK_DEV, dtype=jnp.int32) < shard_count).astype(jnp.int32)
        return jnp.zeros((TOK_DEV,), jnp.int32).at[shuffled].set(chosen)
    full_mask = jax.vmap(shard_mask)(shard_keys, counts).reshape(-1)
    ordering = jnp.argsort(1 - full_mask, stable=True)
    return ordering[:SELECTED_TOKENS].astype(jnp.int32)


def attention_inputs(key):
    base_key = jax.random.fold_in(key, 11)
    key_block_list = jax.random.split(base_key, 3)
    overall_row_count = N_CTX * CAP
    group_count = QUERY_HEADS // KEY_VALUE_HEADS
    unprojected_queries = jnp.clip(jax.random.normal(key_block_list[0], (overall_row_count, KEY_VALUE_HEADS, group_count, HEAD_SIZE), jnp.float32), -6.0, 6.0)
    unprojected_keys = jnp.clip(jax.random.normal(key_block_list[1], (overall_row_count, KEY_VALUE_HEADS, HEAD_SIZE), jnp.float32), -6.0, 6.0)
    unprojected_values = jnp.clip(jax.random.normal(key_block_list[2], (overall_row_count, KEY_VALUE_HEADS, HEAD_SIZE), jnp.float32), -6.0, 6.0)
    queries = unprojected_queries.reshape(overall_row_count, QUERY_HEADS * HEAD_SIZE).astype(jnp.bfloat16)
    stacked_blocks = jnp.concatenate([unprojected_keys.reshape(overall_row_count, KEY_VALUE_HEADS * HEAD_SIZE), unprojected_values.reshape(overall_row_count, KEY_VALUE_HEADS * HEAD_SIZE)], axis=1)
    return (queries, stacked_blocks.astype(jnp.bfloat16))


def draw_queries(key, part):
    return attention_inputs(key)[0]


def draw_keys_values(key, part):
    return attention_inputs(key)[1]


def shard_levels(stream_key, extent, shards, low, high):
    def one(axis_at, shards_of):
        draws = jax.random.uniform(jax.random.fold_in(jax.random.fold_in(stream_key, 6), axis_at), (shards_of,), jnp.float32, low / len(shards), high / len(shards))
        return jnp.repeat(jnp.exp(draws), extent[axis_at] // shards_of).reshape((-1,) + (1,) * (len(extent) - axis_at - 1))

    gain = one(*shards[0])
    for cut in shards[1:]:
        gain = gain * one(*cut)
    return gain


def setup_inputs(seed: int = 0, part: int = 0) -> dict:
    seeds = jax.random.split(jax.random.key(seed), 5)
    part_splits = jax.random.split(jax.random.fold_in(seeds[4], part), 5)
    positions = draw_positions(jax.random.fold_in(jax.random.fold_in(seeds[4], part), 71), part)
    queries = draw_queries(jax.random.fold_in(jax.random.fold_in(seeds[4], part), 71), part)
    keys_values = draw_keys_values(jax.random.fold_in(jax.random.fold_in(seeds[4], part), 71), part)
    router_weight = jnp.clip(jnp.exp(math.log(2.0) - 2.0794415 * jax.random.uniform(part_splits[3], (N_CTX * CAP,), jnp.float32) ** shard_levels(part_splits[3], (N_CTX * CAP,), ((0, 32),), -0.2, 0.2)), 0.25, 2.0).astype(jnp.bfloat16)
    return {"positions": positions, "queries": queries, "keys_values": keys_values, "router_weight": router_weight}


def reference(positions, queries, keys_values, router_weight):
    bounds = jnp.arange(N_CTX + 1, dtype=jnp.int32) * TOK_DEV
    offsets = lax.optimization_barrier(jnp.sum((positions[None, :] < bounds[:, None]).astype(jnp.int32), axis=1)).astype(jnp.int32)
    starts = offsets[:-1]
    counts = offsets[1:] - starts
    global_idx = jnp.arange(SELECTED_TOKENS, dtype=jnp.int32)
    owners = lax.optimization_barrier(jnp.sum((offsets[None, 1:] <= global_idx[:, None]).astype(jnp.int32), axis=1)).astype(jnp.int32)
    source_rows = (owners * CAP + global_idx - jnp.take(starts, owners)).astype(jnp.int32)
    sel_queries = jnp.take(queries, source_rows, axis=0)
    selected_key_value = jnp.take(keys_values, source_rows, axis=0)
    sel_gate = jnp.take(router_weight, source_rows, axis=0)
    group_count = QUERY_HEADS // KEY_VALUE_HEADS
    every_key_row = selected_key_value[:, :KEY_VALUE_HEADS * HEAD_SIZE].reshape(SELECTED_TOKENS, KEY_VALUE_HEADS, HEAD_SIZE).astype(jnp.float32)
    every_value_row = selected_key_value[:, KEY_VALUE_HEADS * HEAD_SIZE:].reshape(SELECTED_TOKENS, KEY_VALUE_HEADS, HEAD_SIZE).astype(jnp.float32)
    query_block_start = math.gcd(SELECTED_TOKENS, 512)
    num_blocks = SELECTED_TOKENS // query_block_start
    score_scale = 1.0 / math.sqrt(HEAD_SIZE)

    def one_block(block_id):
        first = block_id * query_block_start
        query_row_count = lax.dynamic_slice_in_dim(sel_queries, first, query_block_start, 0)
        query_row_count = query_row_count.reshape(query_block_start, KEY_VALUE_HEADS, group_count, HEAD_SIZE).astype(jnp.float32)
        scores = jnp.einsum('qkgd,ckd->kgqc', query_row_count, every_key_row) * score_scale
        query_index = first + jnp.arange(query_block_start, dtype=jnp.int32)
        visible = global_idx[None, :] <= query_index[:, None]
        masked = jnp.where(visible, scores, -1e+30)
        row_max = lax.optimization_barrier(jnp.max(masked, axis=-1))
        weights = jnp.where(visible, jnp.exp(masked - row_max[..., None]), 0.0)
        totals = lax.optimization_barrier(jnp.sum(weights, axis=-1))
        rounded = lax.optimization_barrier(weights.astype(jnp.bfloat16)).astype(jnp.float32)
        weighted = jnp.einsum('kgqc,ckd->qkgd', rounded, every_value_row)
        weighted = weighted / jnp.transpose(totals, (2, 0, 1))[..., None]
        return weighted.reshape(query_block_start, QUERY_HEADS * HEAD_SIZE)
    attended_sel = lax.map(one_block, jnp.arange(num_blocks, dtype=jnp.int32)).reshape(SELECTED_TOKENS, QUERY_HEADS * HEAD_SIZE)
    scaled = sel_gate.astype(jnp.float32)[:, None] * attended_sel
    slot_rows = jnp.arange(N_CTX * CAP, dtype=jnp.int32)
    shard_ids = slot_rows // CAP
    slot_ids = slot_rows % CAP
    live_slot = slot_ids < jnp.take(counts, shard_ids)
    target_rows = jnp.clip(jnp.take(starts, shard_ids) + slot_ids, 0, SELECTED_TOKENS - 1).astype(jnp.int32)
    picked = jnp.take(scaled, target_rows, axis=0)
    return jnp.where(live_slot[:, None], picked, 0.0).astype(jnp.bfloat16)
```

```python
import math

import jax
import jax.numpy as jnp
from jax import lax
from jax.experimental import pallas as pl
from jax.experimental.pallas import tpu as pltpu
from jax.sharding import PartitionSpec as P

QUERY_HEADS = 16
KEY_VALUE_HEADS = 4
HEAD_SIZE = 128
SEL_DEV = 96
TOK_DEV = 768
CAP = 288
KEY_CHUNK = 512


large_negative_fill = -1e30


def shard_offsets(positions, devices_ctx):
    bounds = jnp.arange(devices_ctx + 1, dtype=jnp.int32) * TOK_DEV
    return jnp.sum((positions[None, :] < bounds[:, None]).astype(jnp.int32), axis=1)


def pack_forward(arrays, offsets, my_rank, devices_ctx, pair_slots):
    my_start = offsets[my_rank]
    my_count = offsets[my_rank + 1] - my_start
    target = jnp.arange(devices_ctx, dtype=jnp.int32)[:, None]
    slot_index = jnp.arange(pair_slots, dtype=jnp.int32)[None, :]
    global_idx = (my_start // devices_ctx + slot_index) * devices_ctx + target
    local_idx = global_idx - my_start
    usable = ((local_idx >= 0) & (local_idx < my_count)).reshape(-1)
    picked = jnp.clip(local_idx, 0, CAP - 1).reshape(-1)
    result = []
    for member in arrays:
        gathered_rows = jnp.take(member, picked, axis=0)
        mask_shape = usable.reshape(usable.shape + (1,) * (gathered_rows.ndim - 1))
        gathered_rows = jnp.where(mask_shape, gathered_rows, jnp.zeros_like(gathered_rows))
        result.append(gathered_rows.reshape((devices_ctx, pair_slots) + member.shape[1:]))
    return tuple(result)


def unpack_forward(received, offsets, my_rank, devices_ctx, pair_slots):
    slot_ids = jnp.arange(SEL_DEV, dtype=jnp.int32)
    global_idx = slot_ids * devices_ctx + my_rank
    owners = jnp.sum((offsets[None, 1:] <= global_idx[:, None]).astype(jnp.int32), axis=1)
    slot_index = slot_ids - jnp.take(offsets, owners) // devices_ctx
    picked = owners * pair_slots + slot_index
    return tuple(
        (jnp.take(member.reshape((-1,) + member.shape[2:]), picked, axis=0) for member in received)
    )


def attention_kernel(qidx_ref, kidx_ref, gate_ref, q_ref, k_ref, v_ref, o_ref):
    group_count = QUERY_HEADS // KEY_VALUE_HEADS
    rows = q_ref.shape[0]
    keys = k_ref.shape[0]
    score_scale = 1.0 / math.sqrt(HEAD_SIZE)
    qidx = qidx_ref[...]
    valid = qidx >= 0
    gate = gate_ref[...]
    for g in range(group_count):
        q = q_ref[:, g * HEAD_SIZE : (g + 1) * HEAD_SIZE]
        m_run = jnp.full((rows, 1), large_negative_fill, jnp.float32)
        l_run = jnp.zeros((rows, 1), jnp.float32)
        acc = jnp.zeros((rows, HEAD_SIZE), jnp.float32)
        for c in range(keys // KEY_CHUNK):
            lo = c * KEY_CHUNK
            k = k_ref[lo : lo + KEY_CHUNK, :]
            v = v_ref[lo : lo + KEY_CHUNK, :]
            s = lax.dot_general(
                q, k, (((1,), (1,)), ((), ())), preferred_element_type=jnp.float32
            )
            visible = kidx_ref[:, lo : lo + KEY_CHUNK] <= qidx
            s = jnp.where(visible, s, large_negative_fill)
            m_new = jnp.maximum(m_run, jnp.max(s, axis=-1, keepdims=True))
            p = jnp.exp((s - m_new) * score_scale)
            factor = jnp.exp((m_run - m_new) * score_scale)
            l_run = l_run * factor + jnp.sum(p, axis=-1, keepdims=True)
            acc = acc * factor + jnp.dot(
                p.astype(jnp.bfloat16), v, preferred_element_type=jnp.float32
            )
            m_run = m_new
        out = jnp.where(valid, gate * (acc / l_run), 0.0)
        o_ref[:, g * HEAD_SIZE : (g + 1) * HEAD_SIZE] = out.astype(o_ref.dtype)


def local_attention(qidx, kidx, gate, queries, kv_all):
    rows = queries.shape[0]
    keys = kv_all.shape[0]
    group_width = (QUERY_HEADS // KEY_VALUE_HEADS) * HEAD_SIZE
    return pl.pallas_call(
        attention_kernel,
        grid=(KEY_VALUE_HEADS,),
        in_specs=[
            pl.BlockSpec((rows, 1), lambda h: (0, 0)),
            pl.BlockSpec((1, keys), lambda h: (0, 0)),
            pl.BlockSpec((rows, 1), lambda h: (0, 0)),
            pl.BlockSpec((rows, group_width), lambda h: (0, h)),
            pl.BlockSpec((keys, HEAD_SIZE), lambda h: (0, h)),
            pl.BlockSpec((keys, HEAD_SIZE), lambda h: (0, h + KEY_VALUE_HEADS)),
        ],
        out_specs=pl.BlockSpec((rows, group_width), lambda h: (0, h)),
        out_shape=jax.ShapeDtypeStruct((rows, QUERY_HEADS * HEAD_SIZE), jnp.bfloat16),
        compiler_params=pltpu.CompilerParams(dimension_semantics=("arbitrary",)),
    )(qidx, kidx, gate, queries, kv_all, kv_all)


def per_device(positions, queries, keys_values, router_weight):
    devices_ctx = lax.axis_size("ctx")
    my_rank = lax.axis_index("ctx")
    pair_slots = (CAP + devices_ctx - 1) // devices_ctx + 1
    offsets = shard_offsets(positions, devices_ctx)
    packed = pack_forward((keys_values,), offsets, my_rank, devices_ctx, pair_slots)
    moved = (lax.all_to_all(packed[0], "ctx", split_axis=0, concat_axis=0, tiled=True),)
    (kv_bal,) = unpack_forward(moved, offsets, my_rank, devices_ctx, pair_slots)
    kv_all = lax.all_gather(kv_bal, "ctx", axis=0, tiled=True)
    key_rows = jnp.arange(SEL_DEV * devices_ctx, dtype=jnp.int32)
    kidx = (key_rows % SEL_DEV * devices_ctx + key_rows // SEL_DEV)[None, :]
    my_start = offsets[my_rank]
    my_count = offsets[my_rank + 1] - my_start
    slot_ids = jnp.arange(CAP, dtype=jnp.int32)
    qidx = jnp.where(slot_ids < my_count, my_start + slot_ids, -1)[:, None]
    gate = router_weight.astype(jnp.float32)[:, None]
    return local_attention(qidx, kidx, gate, queries, kv_all)


def solution(mesh):
    in_specs = (P("dp"), P(("dp", "ctx"), None), P(("dp", "ctx"), None), P(("dp", "ctx")))
    out_specs = P(("dp", "ctx"), None)
    return jax.shard_map(
        per_device, mesh=mesh, in_specs=in_specs, out_specs=out_specs, check_vma=False
    )
```

```python
import functools
import math

import jax
import jax.numpy as jnp
from jax import lax
from jax.experimental import pallas as pl
from jax.experimental.pallas import tpu as pltpu
from jax.sharding import PartitionSpec as P

QUERY_HEADS = 16
KEY_VALUE_HEADS = 4
HEAD_SIZE = 128
SEL_DEV = 96
TOK_DEV = 768
CAP = 288
KEY_CHUNK = 512
GATHER_CHUNKS = 3


large_negative_fill = -1e30


def shard_offsets(positions, devices_ctx):
    bounds = jnp.arange(devices_ctx + 1, dtype=jnp.int32) * TOK_DEV
    return jnp.sum((positions[None, :] < bounds[:, None]).astype(jnp.int32), axis=1)


def pack_forward(arrays, offsets, my_rank, devices_ctx, pair_slots):
    my_start = offsets[my_rank]
    my_count = offsets[my_rank + 1] - my_start
    target = jnp.arange(devices_ctx, dtype=jnp.int32)[:, None]
    slot_index = jnp.arange(pair_slots, dtype=jnp.int32)[None, :]
    global_idx = (my_start // devices_ctx + slot_index) * devices_ctx + target
    local_idx = global_idx - my_start
    usable = ((local_idx >= 0) & (local_idx < my_count)).reshape(-1)
    picked = jnp.clip(local_idx, 0, CAP - 1).reshape(-1)
    result = []
    for member in arrays:
        gathered_rows = jnp.take(member, picked, axis=0)
        mask_shape = usable.reshape(usable.shape + (1,) * (gathered_rows.ndim - 1))
        gathered_rows = jnp.where(mask_shape, gathered_rows, jnp.zeros_like(gathered_rows))
        result.append(gathered_rows.reshape((devices_ctx, pair_slots) + member.shape[1:]))
    return tuple(result)


def unpack_forward(received, offsets, my_rank, devices_ctx, pair_slots):
    slot_ids = jnp.arange(SEL_DEV, dtype=jnp.int32)
    global_idx = slot_ids * devices_ctx + my_rank
    owners = jnp.sum((offsets[None, 1:] <= global_idx[:, None]).astype(jnp.int32), axis=1)
    slot_index = slot_ids - jnp.take(offsets, owners) // devices_ctx
    picked = owners * pair_slots + slot_index
    return tuple(
        (jnp.take(member.reshape((-1,) + member.shape[2:]), picked, axis=0) for member in received)
    )


def attention_kernel(first, last, qidx_ref, kidx_ref, gate_ref, q_ref, k_ref, v_ref, *rest):
    group_count = QUERY_HEADS // KEY_VALUE_HEADS
    rows = q_ref.shape[0]
    keys = k_ref.shape[0]
    score_scale = 1.0 / math.sqrt(HEAD_SIZE)
    if first:
        state_in = None
        state_out = rest
    else:
        state_in = rest[:3]
        state_out = rest[3:]
    qidx = qidx_ref[...]
    for g in range(group_count):
        cols = slice(g * HEAD_SIZE, (g + 1) * HEAD_SIZE)
        q = q_ref[:, cols]
        if first:
            m_run = jnp.full((rows, 1), large_negative_fill, jnp.float32)
            l_run = jnp.zeros((rows, 1), jnp.float32)
            acc = jnp.zeros((rows, HEAD_SIZE), jnp.float32)
        else:
            acc = state_in[0][:, cols]
            m_run = state_in[1][0, :, g : g + 1]
            l_run = state_in[2][0, :, g : g + 1]
        for c in range(keys // KEY_CHUNK):
            lo = c * KEY_CHUNK
            k = k_ref[lo : lo + KEY_CHUNK, :]
            v = v_ref[lo : lo + KEY_CHUNK, :]
            s = lax.dot_general(
                q, k, (((1,), (1,)), ((), ())), preferred_element_type=jnp.float32
            )
            visible = kidx_ref[:, lo : lo + KEY_CHUNK] <= qidx
            s = jnp.where(visible, s, large_negative_fill)
            m_new = jnp.maximum(m_run, jnp.max(s, axis=-1, keepdims=True))
            p = jnp.exp((s - m_new) * score_scale)
            factor = jnp.exp((m_run - m_new) * score_scale)
            l_run = l_run * factor + jnp.sum(p, axis=-1, keepdims=True)
            acc = acc * factor + jnp.dot(
                p.astype(jnp.bfloat16), v, preferred_element_type=jnp.float32
            )
            m_run = m_new
        if last:
            out = jnp.where(qidx >= 0, gate_ref[...] * (acc / l_run), 0.0)
            state_out[0][:, cols] = out.astype(state_out[0].dtype)
        else:
            state_out[0][:, cols] = acc
            state_out[1][0, :, g : g + 1] = m_run
            state_out[2][0, :, g : g + 1] = l_run


def local_attention(qidx, kidx, gate, queries, kv_part, state, last):
    rows = queries.shape[0]
    keys = kv_part.shape[0]
    group_count = QUERY_HEADS // KEY_VALUE_HEADS
    group_width = group_count * HEAD_SIZE
    width = QUERY_HEADS * HEAD_SIZE
    acc_spec = pl.BlockSpec((rows, group_width), lambda h: (0, h))
    stat_spec = pl.BlockSpec((1, rows, group_count), lambda h: (h, 0, 0))
    stat_shape = jax.ShapeDtypeStruct((KEY_VALUE_HEADS, rows, group_count), jnp.float32)
    in_specs = [
        pl.BlockSpec((rows, 1), lambda h: (0, 0)),
        pl.BlockSpec((1, keys), lambda h: (0, 0)),
        pl.BlockSpec((rows, 1), lambda h: (0, 0)),
        pl.BlockSpec((rows, group_width), lambda h: (0, h)),
        pl.BlockSpec((keys, HEAD_SIZE), lambda h: (0, h)),
        pl.BlockSpec((keys, HEAD_SIZE), lambda h: (0, h + KEY_VALUE_HEADS)),
    ]
    operands = [qidx, kidx, gate, queries, kv_part, kv_part]
    if state is not None:
        in_specs += [acc_spec, stat_spec, stat_spec]
        operands += list(state)
    if last:
        out_specs = acc_spec
        out_shape = jax.ShapeDtypeStruct((rows, width), jnp.bfloat16)
    else:
        out_specs = (acc_spec, stat_spec, stat_spec)
        out_shape = (jax.ShapeDtypeStruct((rows, width), jnp.float32), stat_shape, stat_shape)
    return pl.pallas_call(
        functools.partial(attention_kernel, state is None, last),
        grid=(KEY_VALUE_HEADS,),
        in_specs=in_specs,
        out_specs=out_specs,
        out_shape=out_shape,
        compiler_params=pltpu.CompilerParams(dimension_semantics=("arbitrary",)),
    )(*operands)


def per_device(positions, queries, keys_values, router_weight):
    devices_ctx = lax.axis_size("ctx")
    my_rank = lax.axis_index("ctx")
    pair_slots = (CAP + devices_ctx - 1) // devices_ctx + 1
    offsets = shard_offsets(positions, devices_ctx)
    packed = pack_forward((keys_values,), offsets, my_rank, devices_ctx, pair_slots)
    moved = (lax.all_to_all(packed[0], "ctx", split_axis=0, concat_axis=0, tiled=True),)
    (kv_bal,) = unpack_forward(moved, offsets, my_rank, devices_ctx, pair_slots)
    my_start = offsets[my_rank]
    my_count = offsets[my_rank + 1] - my_start
    slot_ids = jnp.arange(CAP, dtype=jnp.int32)
    qidx = jnp.where(slot_ids < my_count, my_start + slot_ids, -1)[:, None]
    gate = router_weight.astype(jnp.float32)[:, None]
    chunk_slots = SEL_DEV // GATHER_CHUNKS
    state = None
    for c in range(GATHER_CHUNKS):
        part = kv_bal[c * chunk_slots : (c + 1) * chunk_slots]
        kv_part = lax.all_gather(part, "ctx", axis=0, tiled=True)
        key_rows = jnp.arange(chunk_slots * devices_ctx, dtype=jnp.int32)
        kidx = ((c * chunk_slots + key_rows % chunk_slots) * devices_ctx + key_rows // chunk_slots)[None, :]
        last = c == GATHER_CHUNKS - 1
        state = local_attention(qidx, kidx, gate, queries, kv_part, state, last)
    return state


def solution(mesh):
    in_specs = (P("dp"), P(("dp", "ctx"), None), P(("dp", "ctx"), None), P(("dp", "ctx")))
    out_specs = P(("dp", "ctx"), None)
    return jax.shard_map(
        per_device, mesh=mesh, in_specs=in_specs, out_specs=out_specs, check_vma=False
    )
```

```python
import math

import jax
import jax.numpy as jnp
from jax import lax
from jax.experimental import pallas as pl
from jax.experimental.pallas import tpu as pltpu
from jax.sharding import PartitionSpec as P

QUERY_HEADS = 16
KEY_VALUE_HEADS = 4
HEAD_SIZE = 128
SEL_DEV = 96
TOK_DEV = 768
CAP = 288
KEY_CHUNK = 512
CTX_X = 4


large_negative_fill = -1e30


def shard_offsets(positions, devices_ctx):
    bounds = jnp.arange(devices_ctx + 1, dtype=jnp.int32) * TOK_DEV
    return jnp.sum((positions[None, :] < bounds[:, None]).astype(jnp.int32), axis=1)


def pack_forward(arrays, offsets, my_rank, devices_ctx, pair_slots):
    my_start = offsets[my_rank]
    my_count = offsets[my_rank + 1] - my_start
    target = jnp.arange(devices_ctx, dtype=jnp.int32)[:, None]
    slot_index = jnp.arange(pair_slots, dtype=jnp.int32)[None, :]
    global_idx = (my_start // devices_ctx + slot_index) * devices_ctx + target
    local_idx = global_idx - my_start
    usable = ((local_idx >= 0) & (local_idx < my_count)).reshape(-1)
    picked = jnp.clip(local_idx, 0, CAP - 1).reshape(-1)
    result = []
    for member in arrays:
        gathered_rows = jnp.take(member, picked, axis=0)
        mask_shape = usable.reshape(usable.shape + (1,) * (gathered_rows.ndim - 1))
        gathered_rows = jnp.where(mask_shape, gathered_rows, jnp.zeros_like(gathered_rows))
        result.append(gathered_rows.reshape((devices_ctx, pair_slots) + member.shape[1:]))
    return tuple(result)


def unpack_forward(received, offsets, my_rank, devices_ctx, pair_slots):
    slot_ids = jnp.arange(SEL_DEV, dtype=jnp.int32)
    global_idx = slot_ids * devices_ctx + my_rank
    owners = jnp.sum((offsets[None, 1:] <= global_idx[:, None]).astype(jnp.int32), axis=1)
    slot_index = slot_ids - jnp.take(offsets, owners) // devices_ctx
    picked = owners * pair_slots + slot_index
    return tuple(
        (jnp.take(member.reshape((-1,) + member.shape[2:]), picked, axis=0) for member in received)
    )


def attention_kernel(qidx_ref, kidx_ref, gate_ref, q_ref, k_ref, v_ref, o_ref):
    group_count = QUERY_HEADS // KEY_VALUE_HEADS
    rows = q_ref.shape[0]
    keys = k_ref.shape[0]
    score_scale = 1.0 / math.sqrt(HEAD_SIZE)
    qidx = qidx_ref[...]
    valid = qidx >= 0
    gate = gate_ref[...]
    for g in range(group_count):
        q = q_ref[:, g * HEAD_SIZE : (g + 1) * HEAD_SIZE]
        m_run = jnp.full((rows, 1), large_negative_fill, jnp.float32)
        l_run = jnp.zeros((rows, 1), jnp.float32)
        acc = jnp.zeros((rows, HEAD_SIZE), jnp.float32)
        for c in range(keys // KEY_CHUNK):
            lo = c * KEY_CHUNK
            k = k_ref[lo : lo + KEY_CHUNK, :]
            v = v_ref[lo : lo + KEY_CHUNK, :]
            s = lax.dot_general(
                q, k, (((1,), (1,)), ((), ())), preferred_element_type=jnp.float32
            )
            visible = kidx_ref[:, lo : lo + KEY_CHUNK] <= qidx
            s = jnp.where(visible, s, large_negative_fill)
            m_new = jnp.maximum(m_run, jnp.max(s, axis=-1, keepdims=True))
            p = jnp.exp((s - m_new) * score_scale)
            factor = jnp.exp((m_run - m_new) * score_scale)
            l_run = l_run * factor + jnp.sum(p, axis=-1, keepdims=True)
            acc = acc * factor + jnp.dot(
                p.astype(jnp.bfloat16), v, preferred_element_type=jnp.float32
            )
            m_run = m_new
        out = jnp.where(valid, gate * (acc / l_run), 0.0)
        o_ref[:, g * HEAD_SIZE : (g + 1) * HEAD_SIZE] = out.astype(o_ref.dtype)


def local_attention(qidx, kidx, gate, queries, kv_all):
    rows = queries.shape[0]
    keys = kv_all.shape[0]
    group_width = (QUERY_HEADS // KEY_VALUE_HEADS) * HEAD_SIZE
    return pl.pallas_call(
        attention_kernel,
        grid=(KEY_VALUE_HEADS,),
        in_specs=[
            pl.BlockSpec((rows, 1), lambda h: (0, 0)),
            pl.BlockSpec((1, keys), lambda h: (0, 0)),
            pl.BlockSpec((rows, 1), lambda h: (0, 0)),
            pl.BlockSpec((rows, group_width), lambda h: (0, h)),
            pl.BlockSpec((keys, HEAD_SIZE), lambda h: (0, h)),
            pl.BlockSpec((keys, HEAD_SIZE), lambda h: (0, h + KEY_VALUE_HEADS)),
        ],
        out_specs=pl.BlockSpec((rows, group_width), lambda h: (0, h)),
        out_shape=jax.ShapeDtypeStruct((rows, QUERY_HEADS * HEAD_SIZE), jnp.bfloat16),
        compiler_params=pltpu.CompilerParams(dimension_semantics=("arbitrary",)),
    )(qidx, kidx, gate, queries, kv_all, kv_all)


def per_device(positions, queries, keys_values, router_weight):
    devices_x = lax.axis_size("cx")
    devices_ctx = lax.axis_size("cy") * devices_x
    my_rank = lax.axis_index("cy") * devices_x + lax.axis_index("cx")
    pair_slots = (CAP + devices_ctx - 1) // devices_ctx + 1
    offsets = shard_offsets(positions, devices_ctx)
    packed = pack_forward((keys_values,), offsets, my_rank, devices_ctx, pair_slots)
    moved = (lax.all_to_all(packed[0], ("cy", "cx"), split_axis=0, concat_axis=0, tiled=True),)
    (kv_bal,) = unpack_forward(moved, offsets, my_rank, devices_ctx, pair_slots)
    kv_row = lax.all_gather(kv_bal, "cx", axis=0, tiled=True)
    kv_all = lax.all_gather(kv_row, "cy", axis=0, tiled=True)
    key_rows = jnp.arange(SEL_DEV * devices_ctx, dtype=jnp.int32)
    kidx = (key_rows % SEL_DEV * devices_ctx + key_rows // SEL_DEV)[None, :]
    my_start = offsets[my_rank]
    my_count = offsets[my_rank + 1] - my_start
    slot_ids = jnp.arange(CAP, dtype=jnp.int32)
    qidx = jnp.where(slot_ids < my_count, my_start + slot_ids, -1)[:, None]
    gate = router_weight.astype(jnp.float32)[:, None]
    return local_attention(qidx, kidx, gate, queries, kv_all)


def solution(mesh):
    devices = mesh.devices
    split = jax.sharding.Mesh(
        devices.reshape(devices.shape[0], devices.shape[1] // CTX_X, CTX_X), ("dp", "cy", "cx")
    )
    rows = ("dp", "cy", "cx")
    in_specs = (P("dp"), P(rows, None), P(rows, None), P(rows))
    out_specs = P(rows, None)
    return jax.shard_map(
        per_device, mesh=split, in_specs=in_specs, out_specs=out_specs, check_vma=False
    )
```

```python
import functools
import math

import jax
import jax.numpy as jnp
from jax import lax
from jax.experimental import pallas as pl
from jax.experimental.pallas import tpu as pltpu
from jax.sharding import PartitionSpec as P

QUERY_HEADS = 16
KEY_VALUE_HEADS = 4
HEAD_SIZE = 128
SEL_DEV = 96
TOK_DEV = 768
CAP = 288
KEY_CHUNK = 512
CTX_X = 4


large_negative_fill = -1e30


def shard_offsets(positions, devices_ctx):
    bounds = jnp.arange(devices_ctx + 1, dtype=jnp.int32) * TOK_DEV
    return jnp.sum((positions[None, :] < bounds[:, None]).astype(jnp.int32), axis=1)


def pack_forward(arrays, offsets, my_rank, devices_ctx, pair_slots):
    my_start = offsets[my_rank]
    my_count = offsets[my_rank + 1] - my_start
    target = jnp.arange(devices_ctx, dtype=jnp.int32)[:, None]
    slot_index = jnp.arange(pair_slots, dtype=jnp.int32)[None, :]
    global_idx = (my_start // devices_ctx + slot_index) * devices_ctx + target
    local_idx = global_idx - my_start
    usable = ((local_idx >= 0) & (local_idx < my_count)).reshape(-1)
    picked = jnp.clip(local_idx, 0, CAP - 1).reshape(-1)
    result = []
    for member in arrays:
        gathered_rows = jnp.take(member, picked, axis=0)
        mask_shape = usable.reshape(usable.shape + (1,) * (gathered_rows.ndim - 1))
        gathered_rows = jnp.where(mask_shape, gathered_rows, jnp.zeros_like(gathered_rows))
        result.append(gathered_rows.reshape((devices_ctx, pair_slots) + member.shape[1:]))
    return tuple(result)


def unpack_forward(received, offsets, my_rank, devices_ctx, pair_slots):
    slot_ids = jnp.arange(SEL_DEV, dtype=jnp.int32)
    global_idx = slot_ids * devices_ctx + my_rank
    owners = jnp.sum((offsets[None, 1:] <= global_idx[:, None]).astype(jnp.int32), axis=1)
    slot_index = slot_ids - jnp.take(offsets, owners) // devices_ctx
    picked = owners * pair_slots + slot_index
    return tuple(
        (jnp.take(member.reshape((-1,) + member.shape[2:]), picked, axis=0) for member in received)
    )


def attention_kernel(first, last, n_kv, qidx_ref, kidx_ref, gate_ref, q_ref, *rest):
    group_count = QUERY_HEADS // KEY_VALUE_HEADS
    rows = q_ref.shape[0]
    score_scale = 1.0 / math.sqrt(HEAD_SIZE)
    kv_refs = rest[: 2 * n_kv]
    rest = rest[2 * n_kv :]
    if first:
        state_in = None
        state_out = rest
    else:
        state_in = rest[:3]
        state_out = rest[3:]
    qidx = qidx_ref[...]
    for g in range(group_count):
        cols = slice(g * HEAD_SIZE, (g + 1) * HEAD_SIZE)
        q = q_ref[:, cols]
        if first:
            m_run = jnp.full((rows, 1), large_negative_fill, jnp.float32)
            l_run = jnp.zeros((rows, 1), jnp.float32)
            acc = jnp.zeros((rows, HEAD_SIZE), jnp.float32)
        else:
            acc = state_in[0][:, cols]
            m_run = state_in[1][0, :, g : g + 1]
            l_run = state_in[2][0, :, g : g + 1]
        base = 0
        for i in range(n_kv):
            k = kv_refs[2 * i][...]
            v = kv_refs[2 * i + 1][...]
            keys = k.shape[0]
            s = lax.dot_general(
                q, k, (((1,), (1,)), ((), ())), preferred_element_type=jnp.float32
            )
            visible = kidx_ref[:, base : base + keys] <= qidx
            base += keys
            s = jnp.where(visible, s, large_negative_fill)
            m_new = jnp.maximum(m_run, jnp.max(s, axis=-1, keepdims=True))
            p = jnp.exp((s - m_new) * score_scale)
            factor = jnp.exp((m_run - m_new) * score_scale)
            l_run = l_run * factor + jnp.sum(p, axis=-1, keepdims=True)
            acc = acc * factor + jnp.dot(
                p.astype(jnp.bfloat16), v, preferred_element_type=jnp.float32
            )
            m_run = m_new
        if last:
            out = jnp.where(qidx >= 0, gate_ref[...] * (acc / l_run), 0.0)
            state_out[0][:, cols] = out.astype(state_out[0].dtype)
        else:
            state_out[0][:, cols] = acc
            state_out[1][0, :, g : g + 1] = m_run
            state_out[2][0, :, g : g + 1] = l_run


def local_attention(qidx, kidx, gate, queries, kv_parts, state, last):
    rows = queries.shape[0]
    keys = kidx.shape[1]
    group_count = QUERY_HEADS // KEY_VALUE_HEADS
    group_width = group_count * HEAD_SIZE
    width = QUERY_HEADS * HEAD_SIZE
    acc_spec = pl.BlockSpec((rows, group_width), lambda h: (0, h))
    stat_spec = pl.BlockSpec((1, rows, group_count), lambda h: (h, 0, 0))
    stat_shape = jax.ShapeDtypeStruct((KEY_VALUE_HEADS, rows, group_count), jnp.float32)
    in_specs = [
        pl.BlockSpec((rows, 1), lambda h: (0, 0)),
        pl.BlockSpec((1, keys), lambda h: (0, 0)),
        pl.BlockSpec((rows, 1), lambda h: (0, 0)),
        pl.BlockSpec((rows, group_width), lambda h: (0, h)),
    ]
    operands = [qidx, kidx, gate, queries]
    for part in kv_parts:
        part_rows = part.shape[0]
        in_specs += [
            pl.BlockSpec((part_rows, HEAD_SIZE), lambda h: (0, h)),
            pl.BlockSpec((part_rows, HEAD_SIZE), lambda h: (0, h + KEY_VALUE_HEADS)),
        ]
        operands += [part, part]
    if state is not None:
        in_specs += [acc_spec, stat_spec, stat_spec]
        operands += list(state)
    if last:
        out_specs = acc_spec
        out_shape = jax.ShapeDtypeStruct((rows, width), jnp.bfloat16)
    else:
        out_specs = (acc_spec, stat_spec, stat_spec)
        out_shape = (jax.ShapeDtypeStruct((rows, width), jnp.float32), stat_shape, stat_shape)
    return pl.pallas_call(
        functools.partial(attention_kernel, state is None, last, len(kv_parts)),
        grid=(KEY_VALUE_HEADS,),
        in_specs=in_specs,
        out_specs=out_specs,
        out_shape=out_shape,
        compiler_params=pltpu.CompilerParams(dimension_semantics=("arbitrary",)),
    )(*operands)


def group_key_index(y_row, row_lo, row_count, devices_x, devices_ctx):
    rows = row_lo + jnp.arange(row_count, dtype=jnp.int32)
    source = y_row * devices_x + rows // SEL_DEV
    return rows % SEL_DEV * devices_ctx + source


def per_device(positions, queries, keys_values, router_weight):
    devices_x = lax.axis_size("cx")
    devices_ctx = lax.axis_size("cy") * devices_x
    my_rank = lax.axis_index("cy") * devices_x + lax.axis_index("cx")
    pair_slots = (CAP + devices_ctx - 1) // devices_ctx + 1
    offsets = shard_offsets(positions, devices_ctx)
    packed = pack_forward((keys_values,), offsets, my_rank, devices_ctx, pair_slots)
    moved = (lax.all_to_all(packed[0], ("cy", "cx"), split_axis=0, concat_axis=0, tiled=True),)
    (kv_bal,) = unpack_forward(moved, offsets, my_rank, devices_ctx, pair_slots)
    kv_row = lax.all_gather(kv_bal, "cx", axis=0, tiled=True)
    my_start = offsets[my_rank]
    my_count = offsets[my_rank + 1] - my_start
    slot_ids = jnp.arange(CAP, dtype=jnp.int32)
    qidx = jnp.where(slot_ids < my_count, my_start + slot_ids, -1)[:, None]
    gate = router_weight.astype(jnp.float32)[:, None]
    devices_y = devices_ctx // devices_x
    my_y = lax.axis_index("cy")
    group_rows = kv_row.shape[0]
    half = group_rows // 2
    fwd = [(i, (i + 1) % devices_y) for i in range(devices_y)]
    bwd = [(i, (i - 1) % devices_y) for i in range(devices_y)]

    def kidx_of(pieces):
        return jnp.concatenate(
            [group_key_index(y, lo, n, devices_x, devices_ctx) for y, lo, n in pieces]
        )[None, :]

    state = local_attention(
        qidx, kidx_of([(my_y, 0, group_rows)]), gate, queries, [kv_row], None, False
    )
    ahead = lax.ppermute(kv_row, "cy", fwd)
    behind = lax.ppermute(kv_row, "cy", bwd)
    steps = devices_y // 2

    def ring_step(step, carry):
        ahead, behind, state = carry
        ahead_next = lax.ppermute(ahead, "cy", fwd)
        behind_next = lax.ppermute(behind, "cy", bwd)
        y_a = (my_y - step) % devices_y
        y_b = (my_y + step) % devices_y
        kidx = kidx_of([(y_a, 0, group_rows), (y_b, 0, group_rows)])
        state = local_attention(qidx, kidx, gate, queries, [ahead, behind], state, False)
        return ahead_next, behind_next, state

    ahead, behind, state = lax.fori_loop(1, steps - 1, ring_step, (ahead, behind, state))
    step = steps - 1
    last_a = lax.ppermute(ahead[:half], "cy", fwd)
    last_b = lax.ppermute(behind[half:], "cy", bwd)
    y_a = (my_y - step) % devices_y
    y_b = (my_y + step) % devices_y
    kidx = kidx_of([(y_a, 0, group_rows), (y_b, 0, group_rows)])
    state = local_attention(qidx, kidx, gate, queries, [ahead, behind], state, False)
    y_far = (my_y + steps) % devices_y
    kidx = kidx_of([(y_far, 0, half), (y_far, half, group_rows - half)])
    return local_attention(qidx, kidx, gate, queries, [last_a, last_b], state, True)


def solution(mesh):
    devices = mesh.devices
    split = jax.sharding.Mesh(
        devices.reshape(devices.shape[0], devices.shape[1] // CTX_X, CTX_X), ("dp", "cy", "cx")
    )
    rows = ("dp", "cy", "cx")
    in_specs = (P("dp"), P(rows, None), P(rows, None), P(rows))
    out_specs = P(rows, None)
    return jax.shard_map(
        per_device, mesh=split, in_specs=in_specs, out_specs=out_specs, check_vma=False
    )
```

```python
import functools
import math

import jax
import jax.numpy as jnp
from jax import lax
from jax.experimental import pallas as pl
from jax.experimental.pallas import tpu as pltpu
from jax.sharding import PartitionSpec as P

QUERY_HEADS = 16
KEY_VALUE_HEADS = 4
HEAD_SIZE = 128
SEL_DEV = 96
TOK_DEV = 768
CAP = 288
KEY_CHUNK = 512
CTX_X = 4


large_negative_fill = -1e30


def shard_offsets(positions, devices_ctx):
    bounds = jnp.arange(devices_ctx + 1, dtype=jnp.int32) * TOK_DEV
    return jnp.sum((positions[None, :] < bounds[:, None]).astype(jnp.int32), axis=1)


def pack_forward(arrays, offsets, my_rank, devices_ctx, pair_slots):
    my_start = offsets[my_rank]
    my_count = offsets[my_rank + 1] - my_start
    target = jnp.arange(devices_ctx, dtype=jnp.int32)[:, None]
    slot_index = jnp.arange(pair_slots, dtype=jnp.int32)[None, :]
    global_idx = (my_start // devices_ctx + slot_index) * devices_ctx + target
    local_idx = global_idx - my_start
    usable = ((local_idx >= 0) & (local_idx < my_count)).reshape(-1)
    picked = jnp.clip(local_idx, 0, CAP - 1).reshape(-1)
    result = []
    for member in arrays:
        gathered_rows = jnp.take(member, picked, axis=0)
        mask_shape = usable.reshape(usable.shape + (1,) * (gathered_rows.ndim - 1))
        gathered_rows = jnp.where(mask_shape, gathered_rows, jnp.zeros_like(gathered_rows))
        result.append(gathered_rows.reshape((devices_ctx, pair_slots) + member.shape[1:]))
    return tuple(result)


def unpack_forward(received, offsets, my_rank, devices_ctx, pair_slots):
    slot_ids = jnp.arange(SEL_DEV, dtype=jnp.int32)
    global_idx = slot_ids * devices_ctx + my_rank
    owners = jnp.sum((offsets[None, 1:] <= global_idx[:, None]).astype(jnp.int32), axis=1)
    slot_index = slot_ids - jnp.take(offsets, owners) // devices_ctx
    picked = owners * pair_slots + slot_index
    return tuple(
        (jnp.take(member.reshape((-1,) + member.shape[2:]), picked, axis=0) for member in received)
    )


def attention_kernel(first, last, n_kv, qidx_ref, kidx_ref, gate_ref, q_ref, *rest):
    group_count = QUERY_HEADS // KEY_VALUE_HEADS
    rows = q_ref.shape[0]
    score_scale = 1.0 / math.sqrt(HEAD_SIZE)
    kv_refs = rest[: 2 * n_kv]
    rest = rest[2 * n_kv :]
    if first:
        state_in = None
        state_out = rest
    else:
        state_in = rest[:3]
        state_out = rest[3:]
    qidx = qidx_ref[...]
    for g in range(group_count):
        cols = slice(g * HEAD_SIZE, (g + 1) * HEAD_SIZE)
        q = q_ref[:, cols]
        if first:
            m_run = jnp.full((rows, 1), large_negative_fill, jnp.float32)
            l_run = jnp.zeros((rows, 1), jnp.float32)
            acc = jnp.zeros((rows, HEAD_SIZE), jnp.float32)
        else:
            acc = state_in[0][:, cols]
            m_run = state_in[1][0, :, g : g + 1]
            l_run = state_in[2][0, :, g : g + 1]
        base = 0
        for i in range(n_kv):
            k = kv_refs[2 * i][...]
            v = kv_refs[2 * i + 1][...]
            keys = k.shape[0]
            s = lax.dot_general(
                q, k, (((1,), (1,)), ((), ())), preferred_element_type=jnp.float32
            )
            visible = kidx_ref[:, base : base + keys] <= qidx
            base += keys
            s = jnp.where(visible, s, large_negative_fill)
            m_new = jnp.maximum(m_run, jnp.max(s, axis=-1, keepdims=True))
            p = jnp.exp((s - m_new) * score_scale)
            factor = jnp.exp((m_run - m_new) * score_scale)
            l_run = l_run * factor + jnp.sum(p, axis=-1, keepdims=True)
            acc = acc * factor + jnp.dot(
                p.astype(jnp.bfloat16), v, preferred_element_type=jnp.float32
            )
            m_run = m_new
        if last:
            out = jnp.where(qidx >= 0, gate_ref[...] * (acc / l_run), 0.0)
            state_out[0][:, cols] = out.astype(state_out[0].dtype)
        else:
            state_out[0][:, cols] = acc
            state_out[1][0, :, g : g + 1] = m_run
            state_out[2][0, :, g : g + 1] = l_run


def local_attention(qidx, kidx, gate, queries, kv_parts, state, last):
    rows = queries.shape[0]
    keys = kidx.shape[1]
    group_count = QUERY_HEADS // KEY_VALUE_HEADS
    group_width = group_count * HEAD_SIZE
    width = QUERY_HEADS * HEAD_SIZE
    acc_spec = pl.BlockSpec((rows, group_width), lambda h: (0, h))
    stat_spec = pl.BlockSpec((1, rows, group_count), lambda h: (h, 0, 0))
    stat_shape = jax.ShapeDtypeStruct((KEY_VALUE_HEADS, rows, group_count), jnp.float32)
    in_specs = [
        pl.BlockSpec((rows, 1), lambda h: (0, 0)),
        pl.BlockSpec((1, keys), lambda h: (0, 0)),
        pl.BlockSpec((rows, 1), lambda h: (0, 0)),
        pl.BlockSpec((rows, group_width), lambda h: (0, h)),
    ]
    operands = [qidx, kidx, gate, queries]
    for part in kv_parts:
        part_rows = part.shape[0]
        in_specs += [
            pl.BlockSpec((part_rows, HEAD_SIZE), lambda h: (0, h)),
            pl.BlockSpec((part_rows, HEAD_SIZE), lambda h: (0, h + KEY_VALUE_HEADS)),
        ]
        operands += [part, part]
    if state is not None:
        in_specs += [acc_spec, stat_spec, stat_spec]
        operands += list(state)
    if last:
        out_specs = acc_spec
        out_shape = jax.ShapeDtypeStruct((rows, width), jnp.bfloat16)
    else:
        out_specs = (acc_spec, stat_spec, stat_spec)
        out_shape = (jax.ShapeDtypeStruct((rows, width), jnp.float32), stat_shape, stat_shape)
    return pl.pallas_call(
        functools.partial(attention_kernel, state is None, last, len(kv_parts)),
        grid=(KEY_VALUE_HEADS,),
        in_specs=in_specs,
        out_specs=out_specs,
        out_shape=out_shape,
        compiler_params=pltpu.CompilerParams(dimension_semantics=("arbitrary",)),
    )(*operands)


def group_key_index(y_row, row_lo, row_count, devices_x, devices_ctx):
    rows = row_lo + jnp.arange(row_count, dtype=jnp.int32)
    source = y_row * devices_x + rows // SEL_DEV
    return rows % SEL_DEV * devices_ctx + source


def per_device(positions, queries, keys_values, router_weight):
    devices_x = lax.axis_size("cx")
    devices_ctx = lax.axis_size("cy") * devices_x
    my_rank = lax.axis_index("cy") * devices_x + lax.axis_index("cx")
    pair_slots = (CAP + devices_ctx - 1) // devices_ctx + 1
    offsets = shard_offsets(positions, devices_ctx)
    packed = pack_forward((keys_values,), offsets, my_rank, devices_ctx, pair_slots)
    moved = (lax.all_to_all(packed[0], ("cy", "cx"), split_axis=0, concat_axis=0, tiled=True),)
    (kv_bal,) = unpack_forward(moved, offsets, my_rank, devices_ctx, pair_slots)
    kv_row = lax.all_gather(kv_bal, "cx", axis=0, tiled=True)
    my_start = offsets[my_rank]
    my_count = offsets[my_rank + 1] - my_start
    slot_ids = jnp.arange(CAP, dtype=jnp.int32)
    qidx = jnp.where(slot_ids < my_count, my_start + slot_ids, -1)[:, None]
    gate = router_weight.astype(jnp.float32)[:, None]
    devices_y = devices_ctx // devices_x
    my_y = lax.axis_index("cy")
    group_rows = kv_row.shape[0]
    half = group_rows // 2
    fwd = [(i, (i + 1) % devices_y) for i in range(devices_y)]
    bwd = [(i, (i - 1) % devices_y) for i in range(devices_y)]

    def kidx_of(pieces):
        return jnp.concatenate(
            [group_key_index(y, lo, n, devices_x, devices_ctx) for y, lo, n in pieces]
        )[None, :]

    first = local_attention(
        qidx, kidx_of([(my_y, 0, group_rows)]), gate, queries, [kv_row], None, False
    )
    ahead = lax.ppermute(kv_row, "cy", fwd)
    behind = lax.ppermute(kv_row, "cy", bwd)
    steps = devices_y // 2

    def ring_step(carry, step):
        ahead, behind = carry
        ahead_next = lax.ppermute(ahead, "cy", fwd)
        behind_next = lax.ppermute(behind, "cy", bwd)
        y_a = (my_y - step) % devices_y
        y_b = (my_y + step) % devices_y
        kidx = kidx_of([(y_a, 0, group_rows), (y_b, 0, group_rows)])
        part = local_attention(qidx, kidx, gate, queries, [ahead, behind], None, False)
        return (ahead_next, behind_next), part

    (ahead, behind), looped = lax.scan(
        ring_step, (ahead, behind), jnp.arange(1, steps - 1, dtype=jnp.int32)
    )
    step = steps - 1
    last_a = lax.ppermute(ahead[:half], "cy", fwd)
    last_b = lax.ppermute(behind[half:], "cy", bwd)
    y_a = (my_y - step) % devices_y
    y_b = (my_y + step) % devices_y
    kidx = kidx_of([(y_a, 0, group_rows), (y_b, 0, group_rows)])
    third = local_attention(qidx, kidx, gate, queries, [ahead, behind], None, False)
    y_far = (my_y + steps) % devices_y
    kidx = kidx_of([(y_far, 0, half), (y_far, half, group_rows - half)])
    fourth = local_attention(qidx, kidx, gate, queries, [last_a, last_b], None, False)
    parts = [first, third, fourth]
    acc_all = jnp.concatenate([looped[0]] + [p[0][None] for p in parts])
    m_all = jnp.concatenate([looped[1]] + [p[1][None] for p in parts])
    l_all = jnp.concatenate([looped[2]] + [p[2][None] for p in parts])
    return combine(acc_all, m_all, l_all, qidx, gate)


def combine(acc_all, m_all, l_all, qidx, gate):
    count, rows = acc_all.shape[0], acc_all.shape[1]
    score_scale = 1.0 / math.sqrt(HEAD_SIZE)
    m_heads = jnp.transpose(m_all, (0, 2, 1, 3)).reshape(count, rows, QUERY_HEADS)
    l_heads = jnp.transpose(l_all, (0, 2, 1, 3)).reshape(count, rows, QUERY_HEADS)
    m_top = jnp.max(m_heads, axis=0)
    weight = jnp.exp((m_heads - m_top[None]) * score_scale)
    total = jnp.sum(l_heads * weight, axis=0)
    acc = acc_all.reshape(count, rows, QUERY_HEADS, HEAD_SIZE)
    acc = jnp.sum(acc * weight[..., None], axis=0)
    mixed = (acc / total[..., None]).reshape(rows, QUERY_HEADS * HEAD_SIZE)
    return jnp.where(qidx >= 0, gate * mixed, 0.0).astype(jnp.bfloat16)


def solution(mesh):
    devices = mesh.devices
    split = jax.sharding.Mesh(
        devices.reshape(devices.shape[0], devices.shape[1] // CTX_X, CTX_X), ("dp", "cy", "cx")
    )
    rows = ("dp", "cy", "cx")
    in_specs = (P("dp"), P(rows, None), P(rows, None), P(rows))
    out_specs = P(rows, None)
    return jax.shard_map(
        per_device, mesh=split, in_specs=in_specs, out_specs=out_specs, check_vma=False
    )
```

```python
import math

import jax
import jax.numpy as jnp
from jax import lax
from jax.experimental import pallas as pl
from jax.experimental.pallas import tpu as pltpu
from jax.sharding import PartitionSpec as P

QUERY_HEADS = 16
KEY_VALUE_HEADS = 4
HEAD_SIZE = 128
SEL_DEV = 96
TOK_DEV = 768
CAP = 288
KEY_TILE = 256
ROW_TILE = 96
CTX_X = 4


large_negative_fill = -1e30


def shard_offsets(positions, devices_ctx):
    bounds = jnp.arange(devices_ctx + 1, dtype=jnp.int32) * TOK_DEV
    return jnp.sum((positions[None, :] < bounds[:, None]).astype(jnp.int32), axis=1)


def pack_forward(arrays, offsets, my_rank, devices_ctx, pair_slots):
    my_start = offsets[my_rank]
    my_count = offsets[my_rank + 1] - my_start
    target = jnp.arange(devices_ctx, dtype=jnp.int32)[:, None]
    slot_index = jnp.arange(pair_slots, dtype=jnp.int32)[None, :]
    global_idx = (my_start // devices_ctx + slot_index) * devices_ctx + target
    local_idx = global_idx - my_start
    usable = ((local_idx >= 0) & (local_idx < my_count)).reshape(-1)
    picked = jnp.clip(local_idx, 0, CAP - 1).reshape(-1)
    result = []
    for member in arrays:
        gathered_rows = jnp.take(member, picked, axis=0)
        mask_shape = usable.reshape(usable.shape + (1,) * (gathered_rows.ndim - 1))
        gathered_rows = jnp.where(mask_shape, gathered_rows, jnp.zeros_like(gathered_rows))
        result.append(gathered_rows.reshape((devices_ctx, pair_slots) + member.shape[1:]))
    return tuple(result)


def unpack_forward(received, offsets, my_rank, devices_ctx, pair_slots):
    slot_ids = jnp.arange(SEL_DEV, dtype=jnp.int32)
    global_idx = slot_ids * devices_ctx + my_rank
    owners = jnp.sum((offsets[None, 1:] <= global_idx[:, None]).astype(jnp.int32), axis=1)
    slot_index = slot_ids - jnp.take(offsets, owners) // devices_ctx
    picked = owners * pair_slots + slot_index
    return tuple(
        (jnp.take(member.reshape((-1,) + member.shape[2:]), picked, axis=0) for member in received)
    )


def attention_kernel(qidx_ref, kidx_ref, gate_ref, q_ref, k_ref, v_ref, o_ref):
    group_count = QUERY_HEADS // KEY_VALUE_HEADS
    rows = q_ref.shape[0]
    tiles = kidx_ref.shape[0]
    score_scale = 1.0 / math.sqrt(HEAD_SIZE)
    for r in range(rows // ROW_TILE):
        row_sel = slice(r * ROW_TILE, (r + 1) * ROW_TILE)
        qidx = qidx_ref[row_sel, :]
        for g in range(group_count):
            cols = slice(g * HEAD_SIZE, (g + 1) * HEAD_SIZE)
            q = q_ref[row_sel, cols]

            def body(c, carry):
                m_run, l_run, acc = carry
                lo = pl.multiple_of(c * KEY_TILE, KEY_TILE)
                k = k_ref[pl.ds(lo, KEY_TILE), :]
                v = v_ref[pl.ds(lo, KEY_TILE), :]
                s = lax.dot_general(
                    q, k, (((1,), (1,)), ((), ())), preferred_element_type=jnp.float32
                )
                visible = kidx_ref[c] <= qidx
                s = jnp.where(visible, s, large_negative_fill)
                m_new = jnp.maximum(m_run, jnp.max(s, axis=-1, keepdims=True))
                p = jnp.exp((s - m_new) * score_scale)
                factor = jnp.exp((m_run - m_new) * score_scale)
                l_run = l_run * factor + jnp.sum(p, axis=-1, keepdims=True)
                acc = acc * factor + jnp.dot(
                    p.astype(jnp.bfloat16), v, preferred_element_type=jnp.float32
                )
                return m_new, l_run, acc

            init = (
                jnp.full((ROW_TILE, 1), large_negative_fill, jnp.float32),
                jnp.zeros((ROW_TILE, 1), jnp.float32),
                jnp.zeros((ROW_TILE, HEAD_SIZE), jnp.float32),
            )
            m_run, l_run, acc = lax.fori_loop(0, tiles, body, init, unroll=2)
            out = jnp.where(qidx >= 0, gate_ref[row_sel, :] * (acc / l_run), 0.0)
            o_ref[row_sel, cols] = out.astype(o_ref.dtype)


def local_attention(qidx, kidx, gate, queries, kv_all):
    rows = queries.shape[0]
    keys = kv_all.shape[0]
    tiles = keys // KEY_TILE
    group_width = (QUERY_HEADS // KEY_VALUE_HEADS) * HEAD_SIZE
    kidx_tiles = kidx.reshape(tiles, 1, KEY_TILE)
    return pl.pallas_call(
        attention_kernel,
        grid=(KEY_VALUE_HEADS,),
        in_specs=[
            pl.BlockSpec((rows, 1), lambda h: (0, 0)),
            pl.BlockSpec((tiles, 1, KEY_TILE), lambda h: (0, 0, 0)),
            pl.BlockSpec((rows, 1), lambda h: (0, 0)),
            pl.BlockSpec((rows, group_width), lambda h: (0, h)),
            pl.BlockSpec((keys, HEAD_SIZE), lambda h: (0, h)),
            pl.BlockSpec((keys, HEAD_SIZE), lambda h: (0, h + KEY_VALUE_HEADS)),
        ],
        out_specs=pl.BlockSpec((rows, group_width), lambda h: (0, h)),
        out_shape=jax.ShapeDtypeStruct((rows, QUERY_HEADS * HEAD_SIZE), jnp.bfloat16),
        compiler_params=pltpu.CompilerParams(dimension_semantics=("arbitrary",)),
    )(qidx, kidx_tiles, gate, queries, kv_all, kv_all)


def per_device(positions, queries, keys_values, router_weight):
    devices_x = lax.axis_size("cx")
    devices_ctx = lax.axis_size("cy") * devices_x
    my_rank = lax.axis_index("cy") * devices_x + lax.axis_index("cx")
    pair_slots = (CAP + devices_ctx - 1) // devices_ctx + 1
    offsets = shard_offsets(positions, devices_ctx)
    packed = pack_forward((keys_values,), offsets, my_rank, devices_ctx, pair_slots)
    moved = (lax.all_to_all(packed[0], ("cy", "cx"), split_axis=0, concat_axis=0, tiled=True),)
    (kv_bal,) = unpack_forward(moved, offsets, my_rank, devices_ctx, pair_slots)
    kv_row = lax.all_gather(kv_bal, "cx", axis=0, tiled=True)
    kv_all = lax.all_gather(kv_row, "cy", axis=0, tiled=True)
    key_rows = jnp.arange(SEL_DEV * devices_ctx, dtype=jnp.int32)
    kidx = (key_rows % SEL_DEV * devices_ctx + key_rows // SEL_DEV)[None, :]
    my_start = offsets[my_rank]
    my_count = offsets[my_rank + 1] - my_start
    slot_ids = jnp.arange(CAP, dtype=jnp.int32)
    qidx = jnp.where(slot_ids < my_count, my_start + slot_ids, -1)[:, None]
    gate = router_weight.astype(jnp.float32)[:, None]
    return local_attention(qidx, kidx, gate, queries, kv_all)


def solution(mesh):
    devices = mesh.devices
    split = jax.sharding.Mesh(
        devices.reshape(devices.shape[0], devices.shape[1] // CTX_X, CTX_X), ("dp", "cy", "cx")
    )
    rows = ("dp", "cy", "cx")
    in_specs = (P("dp"), P(rows, None), P(rows, None), P(rows))
    out_specs = P(rows, None)
    return jax.shard_map(
        per_device, mesh=split, in_specs=in_specs, out_specs=out_specs, check_vma=False
    )
```

```python
import math

import jax
import jax.numpy as jnp
from jax import lax
from jax.experimental import pallas as pl
from jax.experimental.pallas import tpu as pltpu
from jax.sharding import PartitionSpec as P

QUERY_HEADS = 16
KEY_VALUE_HEADS = 4
HEAD_SIZE = 128
SEL_DEV = 96
TOK_DEV = 768
CAP = 288
KEY_CHUNK = 3072
CTX_X = 4


large_negative_fill = -1e30


def shard_offsets(positions, devices_ctx):
    bounds = jnp.arange(devices_ctx + 1, dtype=jnp.int32) * TOK_DEV
    return jnp.sum((positions[None, :] < bounds[:, None]).astype(jnp.int32), axis=1)


def pack_forward(arrays, offsets, my_rank, devices_ctx, pair_slots):
    my_start = offsets[my_rank]
    my_count = offsets[my_rank + 1] - my_start
    target = jnp.arange(devices_ctx, dtype=jnp.int32)[:, None]
    slot_index = jnp.arange(pair_slots, dtype=jnp.int32)[None, :]
    global_idx = (my_start // devices_ctx + slot_index) * devices_ctx + target
    local_idx = global_idx - my_start
    usable = ((local_idx >= 0) & (local_idx < my_count)).reshape(-1)
    picked = jnp.clip(local_idx, 0, CAP - 1).reshape(-1)
    result = []
    for member in arrays:
        gathered_rows = jnp.take(member, picked, axis=0)
        mask_shape = usable.reshape(usable.shape + (1,) * (gathered_rows.ndim - 1))
        gathered_rows = jnp.where(mask_shape, gathered_rows, jnp.zeros_like(gathered_rows))
        result.append(gathered_rows.reshape((devices_ctx, pair_slots) + member.shape[1:]))
    return tuple(result)


def unpack_forward(received, offsets, my_rank, devices_ctx, pair_slots):
    slot_ids = jnp.arange(SEL_DEV, dtype=jnp.int32)
    global_idx = slot_ids * devices_ctx + my_rank
    owners = jnp.sum((offsets[None, 1:] <= global_idx[:, None]).astype(jnp.int32), axis=1)
    slot_index = slot_ids - jnp.take(offsets, owners) // devices_ctx
    picked = owners * pair_slots + slot_index
    return tuple(
        (jnp.take(member.reshape((-1,) + member.shape[2:]), picked, axis=0) for member in received)
    )


def attention_kernel(qidx_ref, kidx_ref, gate_ref, q_ref, k_ref, v_ref, o_ref):
    group_count = QUERY_HEADS // KEY_VALUE_HEADS
    rows = q_ref.shape[0]
    keys = k_ref.shape[0]
    score_scale = 1.0 / math.sqrt(HEAD_SIZE)
    qidx = qidx_ref[...]
    valid = qidx >= 0
    gate = gate_ref[...]
    for g in range(group_count):
        q = q_ref[:, g * HEAD_SIZE : (g + 1) * HEAD_SIZE]
        m_run = jnp.full((rows, 1), large_negative_fill, jnp.float32)
        l_run = jnp.zeros((rows, 1), jnp.float32)
        acc = jnp.zeros((rows, HEAD_SIZE), jnp.float32)
        for c in range(keys // KEY_CHUNK):
            lo = c * KEY_CHUNK
            k = k_ref[lo : lo + KEY_CHUNK, :]
            v = v_ref[lo : lo + KEY_CHUNK, :]
            s = lax.dot_general(
                q, k, (((1,), (1,)), ((), ())), preferred_element_type=jnp.float32
            )
            visible = kidx_ref[:, lo : lo + KEY_CHUNK] <= qidx
            s = jnp.where(visible, s, large_negative_fill)
            m_new = jnp.maximum(m_run, jnp.max(s, axis=-1, keepdims=True))
            p = jnp.exp((s - m_new) * score_scale)
            factor = jnp.exp((m_run - m_new) * score_scale)
            l_run = l_run * factor + jnp.sum(p, axis=-1, keepdims=True)
            acc = acc * factor + jnp.dot(
                p.astype(jnp.bfloat16), v, preferred_element_type=jnp.float32
            )
            m_run = m_new
        out = jnp.where(valid, gate * (acc / l_run), 0.0)
        o_ref[:, g * HEAD_SIZE : (g + 1) * HEAD_SIZE] = out.astype(o_ref.dtype)


def local_attention(qidx, kidx, gate, queries, kv_all):
    rows = queries.shape[0]
    keys = kv_all.shape[0]
    group_width = (QUERY_HEADS // KEY_VALUE_HEADS) * HEAD_SIZE
    return pl.pallas_call(
        attention_kernel,
        grid=(KEY_VALUE_HEADS,),
        in_specs=[
            pl.BlockSpec((rows, 1), lambda h: (0, 0)),
            pl.BlockSpec((1, keys), lambda h: (0, 0)),
            pl.BlockSpec((rows, 1), lambda h: (0, 0)),
            pl.BlockSpec((rows, group_width), lambda h: (0, h)),
            pl.BlockSpec((keys, HEAD_SIZE), lambda h: (0, h)),
            pl.BlockSpec((keys, HEAD_SIZE), lambda h: (0, h + KEY_VALUE_HEADS)),
        ],
        out_specs=pl.BlockSpec((rows, group_width), lambda h: (0, h)),
        out_shape=jax.ShapeDtypeStruct((rows, QUERY_HEADS * HEAD_SIZE), jnp.bfloat16),
        compiler_params=pltpu.CompilerParams(dimension_semantics=("arbitrary",)),
    )(qidx, kidx, gate, queries, kv_all, kv_all)


def per_device(positions, queries, keys_values, router_weight):
    devices_x = lax.axis_size("cx")
    devices_ctx = lax.axis_size("cy") * devices_x
    my_rank = lax.axis_index("cy") * devices_x + lax.axis_index("cx")
    pair_slots = (CAP + devices_ctx - 1) // devices_ctx + 1
    offsets = shard_offsets(positions, devices_ctx)
    packed = pack_forward((keys_values,), offsets, my_rank, devices_ctx, pair_slots)
    moved = (lax.all_to_all(packed[0], ("cy", "cx"), split_axis=0, concat_axis=0, tiled=True),)
    (kv_bal,) = unpack_forward(moved, offsets, my_rank, devices_ctx, pair_slots)
    kv_row = lax.all_gather(kv_bal, "cx", axis=0, tiled=True)
    kv_all = lax.all_gather(kv_row, "cy", axis=0, tiled=True)
    key_rows = jnp.arange(SEL_DEV * devices_ctx, dtype=jnp.int32)
    kidx = (key_rows % SEL_DEV * devices_ctx + key_rows // SEL_DEV)[None, :]
    my_start = offsets[my_rank]
    my_count = offsets[my_rank + 1] - my_start
    slot_ids = jnp.arange(CAP, dtype=jnp.int32)
    qidx = jnp.where(slot_ids < my_count, my_start + slot_ids, -1)[:, None]
    gate = router_weight.astype(jnp.float32)[:, None]
    return local_attention(qidx, kidx, gate, queries, kv_all)


def solution(mesh):
    devices = mesh.devices
    split = jax.sharding.Mesh(
        devices.reshape(devices.shape[0], devices.shape[1] // CTX_X, CTX_X), ("dp", "cy", "cx")
    )
    rows = ("dp", "cy", "cx")
    in_specs = (P("dp"), P(rows, None), P(rows, None), P(rows))
    out_specs = P(rows, None)
    return jax.shard_map(
        per_device, mesh=split, in_specs=in_specs, out_specs=out_specs, check_vma=False
    )
```

```python
import math

import jax
import jax.numpy as jnp
from jax import lax
from jax.experimental import pallas as pl
from jax.experimental.pallas import tpu as pltpu
from jax.sharding import PartitionSpec as P

QUERY_HEADS = 16
KEY_VALUE_HEADS = 4
HEAD_SIZE = 128
SEL_DEV = 96
TOK_DEV = 768
CAP = 288
KEY_CHUNK = 3072
CTX_X = 4


large_negative_fill = -1e30


def shard_offsets(positions, devices_ctx):
    bounds = jnp.arange(devices_ctx + 1, dtype=jnp.int32) * TOK_DEV
    return jnp.sum((positions[None, :] < bounds[:, None]).astype(jnp.int32), axis=1)


def pack_forward(arrays, offsets, my_rank, devices_ctx, pair_slots):
    my_start = offsets[my_rank]
    my_count = offsets[my_rank + 1] - my_start
    target = jnp.arange(devices_ctx, dtype=jnp.int32)[:, None]
    slot_index = jnp.arange(pair_slots, dtype=jnp.int32)[None, :]
    global_idx = (my_start // devices_ctx + slot_index) * devices_ctx + target
    local_idx = global_idx - my_start
    usable = ((local_idx >= 0) & (local_idx < my_count)).reshape(-1)
    picked = jnp.clip(local_idx, 0, CAP - 1).reshape(-1)
    result = []
    for member in arrays:
        gathered_rows = jnp.take(member, picked, axis=0)
        mask_shape = usable.reshape(usable.shape + (1,) * (gathered_rows.ndim - 1))
        gathered_rows = jnp.where(mask_shape, gathered_rows, jnp.zeros_like(gathered_rows))
        result.append(gathered_rows.reshape((devices_ctx, pair_slots) + member.shape[1:]))
    return tuple(result)


def unpack_forward(received, offsets, my_rank, devices_ctx, pair_slots):
    slot_ids = jnp.arange(SEL_DEV, dtype=jnp.int32)
    global_idx = slot_ids * devices_ctx + my_rank
    owners = jnp.sum((offsets[None, 1:] <= global_idx[:, None]).astype(jnp.int32), axis=1)
    slot_index = slot_ids - jnp.take(offsets, owners) // devices_ctx
    picked = owners * pair_slots + slot_index
    return tuple(
        (jnp.take(member.reshape((-1,) + member.shape[2:]), picked, axis=0) for member in received)
    )


def attention_kernel(qidx_ref, kidx_ref, gate_ref, q_ref, k_ref, v_ref, o_ref):
    group_count = QUERY_HEADS // KEY_VALUE_HEADS
    rows = q_ref.shape[0]
    keys = k_ref.shape[0]
    score_scale = 1.0 / math.sqrt(HEAD_SIZE)
    qidx = qidx_ref[...]
    valid = qidx >= 0
    gate = gate_ref[...]
    for g in range(group_count):
        q = q_ref[:, g * HEAD_SIZE : (g + 1) * HEAD_SIZE]
        m_run = jnp.full((rows, 1), large_negative_fill, jnp.float32)
        l_run = jnp.zeros((rows, 1), jnp.float32)
        acc = jnp.zeros((rows, HEAD_SIZE), jnp.float32)
        for c in range(keys // KEY_CHUNK):
            lo = c * KEY_CHUNK
            k = k_ref[lo : lo + KEY_CHUNK, :]
            v = v_ref[lo : lo + KEY_CHUNK, :]
            s = lax.dot_general(
                q, k, (((1,), (1,)), ((), ())), preferred_element_type=jnp.float32
            )
            visible = kidx_ref[:, lo : lo + KEY_CHUNK] <= qidx
            s = jnp.where(visible, s, large_negative_fill)
            m_new = jnp.maximum(m_run, jnp.max(s, axis=-1, keepdims=True))
            p = jnp.exp((s - m_new) * score_scale)
            factor = jnp.exp((m_run - m_new) * score_scale)
            l_run = l_run * factor + jnp.sum(p, axis=-1, keepdims=True)
            acc = acc * factor + jnp.dot(
                p.astype(jnp.bfloat16), v, preferred_element_type=jnp.float32
            )
            m_run = m_new
        out = jnp.where(valid, gate * (acc / l_run), 0.0)
        o_ref[:, g * HEAD_SIZE : (g + 1) * HEAD_SIZE] = out.astype(o_ref.dtype)


def local_attention(qidx, kidx, gate, queries, kv_all):
    rows = queries.shape[0]
    keys = kv_all.shape[0]
    group_width = (QUERY_HEADS // KEY_VALUE_HEADS) * HEAD_SIZE
    return pl.pallas_call(
        attention_kernel,
        grid=(KEY_VALUE_HEADS,),
        in_specs=[
            pl.BlockSpec((rows, 1), lambda h: (0, 0)),
            pl.BlockSpec((1, keys), lambda h: (0, 0)),
            pl.BlockSpec((rows, 1), lambda h: (0, 0)),
            pl.BlockSpec((rows, group_width), lambda h: (0, h)),
            pl.BlockSpec((keys, HEAD_SIZE), lambda h: (0, h)),
            pl.BlockSpec((keys, HEAD_SIZE), lambda h: (0, h + KEY_VALUE_HEADS)),
        ],
        out_specs=pl.BlockSpec((rows, group_width), lambda h: (0, h)),
        out_shape=jax.ShapeDtypeStruct((rows, QUERY_HEADS * HEAD_SIZE), jnp.bfloat16),
        compiler_params=pltpu.CompilerParams(dimension_semantics=("arbitrary",)),
    )(qidx, kidx, gate, queries, kv_all, kv_all)


def per_device(positions, queries, keys_values, router_weight):
    devices_x = lax.axis_size("cx")
    devices_ctx = lax.axis_size("cy") * devices_x
    my_rank = lax.axis_index("cy") * devices_x + lax.axis_index("cx")
    pair_slots = (CAP + devices_ctx - 1) // devices_ctx + 1
    offsets = shard_offsets(positions, devices_ctx)
    packed = pack_forward((keys_values,), offsets, my_rank, devices_ctx, pair_slots)
    moved = (lax.all_to_all(packed[0], ("cy", "cx"), split_axis=0, concat_axis=0, tiled=True),)
    (kv_bal,) = unpack_forward(moved, offsets, my_rank, devices_ctx, pair_slots)
    kv_row = lax.all_gather(kv_bal, "cx", axis=0, tiled=True)
    devices_y = devices_ctx // devices_x
    my_y = lax.axis_index("cy")
    group_rows = kv_row.shape[0]
    half = group_rows // 2
    fwd = [(i, (i + 1) % devices_y) for i in range(devices_y)]
    bwd = [(i, (i - 1) % devices_y) for i in range(devices_y)]
    parts = [kv_row]
    pieces = [(my_y, 0, group_rows)]
    ahead = kv_row
    behind = kv_row
    steps = devices_y // 2
    for step in range(1, steps):
        ahead = lax.ppermute(ahead, "cy", fwd)
        behind = lax.ppermute(behind, "cy", bwd)
        parts += [ahead, behind]
        pieces += [((my_y - step) % devices_y, 0, group_rows), ((my_y + step) % devices_y, 0, group_rows)]
    parts.append(lax.ppermute(ahead[:half], "cy", fwd))
    parts.append(lax.ppermute(behind[half:], "cy", bwd))
    y_far = (my_y + steps) % devices_y
    pieces += [(y_far, 0, half), (y_far, half, group_rows - half)]
    kv_all = jnp.concatenate(parts, axis=0)
    kidx = jnp.concatenate(
        [group_key_index(y, lo, n, devices_x, devices_ctx) for y, lo, n in pieces]
    )[None, :]
    my_start = offsets[my_rank]
    my_count = offsets[my_rank + 1] - my_start
    slot_ids = jnp.arange(CAP, dtype=jnp.int32)
    qidx = jnp.where(slot_ids < my_count, my_start + slot_ids, -1)[:, None]
    gate = router_weight.astype(jnp.float32)[:, None]
    return local_attention(qidx, kidx, gate, queries, kv_all)


def group_key_index(y_row, row_lo, row_count, devices_x, devices_ctx):
    rows = row_lo + jnp.arange(row_count, dtype=jnp.int32)
    source = y_row * devices_x + rows // SEL_DEV
    return rows % SEL_DEV * devices_ctx + source


def solution(mesh):
    devices = mesh.devices
    split = jax.sharding.Mesh(
        devices.reshape(devices.shape[0], devices.shape[1] // CTX_X, CTX_X), ("dp", "cy", "cx")
    )
    rows = ("dp", "cy", "cx")
    in_specs = (P("dp"), P(rows, None), P(rows, None), P(rows))
    out_specs = P(rows, None)
    return jax.shard_map(
        per_device, mesh=split, in_specs=in_specs, out_specs=out_specs, check_vma=False
    )
```

```python
import math

import jax
import jax.numpy as jnp
from jax import lax
from jax.experimental import pallas as pl
from jax.experimental.pallas import tpu as pltpu
from jax.sharding import PartitionSpec as P

QUERY_HEADS = 16
KEY_VALUE_HEADS = 4
HEAD_SIZE = 128
SEL_DEV = 96
TOK_DEV = 768
CAP = 288
KEY_CHUNK = 3072
CTX_X = 4


large_negative_fill = -1e30


def shard_offsets(positions, devices_ctx):
    bounds = jnp.arange(devices_ctx + 1, dtype=jnp.int32) * TOK_DEV
    return jnp.sum((positions[None, :] < bounds[:, None]).astype(jnp.int32), axis=1)


def pack_forward(arrays, offsets, my_rank, devices_ctx, pair_slots):
    my_start = offsets[my_rank]
    my_count = offsets[my_rank + 1] - my_start
    target = jnp.arange(devices_ctx, dtype=jnp.int32)[:, None]
    slot_index = jnp.arange(pair_slots, dtype=jnp.int32)[None, :]
    global_idx = (my_start // devices_ctx + slot_index) * devices_ctx + target
    local_idx = global_idx - my_start
    usable = ((local_idx >= 0) & (local_idx < my_count)).reshape(-1)
    picked = jnp.clip(local_idx, 0, CAP - 1).reshape(-1)
    result = []
    for member in arrays:
        gathered_rows = jnp.take(member, picked, axis=0)
        mask_shape = usable.reshape(usable.shape + (1,) * (gathered_rows.ndim - 1))
        gathered_rows = jnp.where(mask_shape, gathered_rows, jnp.zeros_like(gathered_rows))
        result.append(gathered_rows.reshape((devices_ctx, pair_slots) + member.shape[1:]))
    return tuple(result)


def unpack_forward(received, offsets, my_rank, devices_ctx, pair_slots):
    slot_ids = jnp.arange(SEL_DEV, dtype=jnp.int32)
    global_idx = slot_ids * devices_ctx + my_rank
    owners = jnp.sum((offsets[None, 1:] <= global_idx[:, None]).astype(jnp.int32), axis=1)
    slot_index = slot_ids - jnp.take(offsets, owners) // devices_ctx
    picked = owners * pair_slots + slot_index
    return tuple(
        (jnp.take(member.reshape((-1,) + member.shape[2:]), picked, axis=0) for member in received)
    )


def attention_kernel(qidx_ref, kidx_ref, gate_ref, q_ref, k_ref, v_ref, o_ref):
    group_count = QUERY_HEADS // KEY_VALUE_HEADS
    rows = q_ref.shape[0]
    keys = k_ref.shape[0]
    score_scale = 1.0 / math.sqrt(HEAD_SIZE)
    qidx = qidx_ref[...]
    valid = qidx >= 0
    gate = gate_ref[...]
    for g in range(group_count):
        q = q_ref[:, g * HEAD_SIZE : (g + 1) * HEAD_SIZE]
        m_run = jnp.full((rows, 1), large_negative_fill, jnp.float32)
        l_run = jnp.zeros((rows, 1), jnp.float32)
        acc = jnp.zeros((rows, HEAD_SIZE), jnp.float32)
        for c in range(keys // KEY_CHUNK):
            lo = c * KEY_CHUNK
            k = k_ref[lo : lo + KEY_CHUNK, :]
            v = v_ref[lo : lo + KEY_CHUNK, :]
            s = lax.dot_general(
                q, k, (((1,), (1,)), ((), ())), preferred_element_type=jnp.float32
            )
            visible = kidx_ref[:, lo : lo + KEY_CHUNK] <= qidx
            s = jnp.where(visible, s, large_negative_fill)
            m_new = jnp.maximum(m_run, jnp.max(s, axis=-1, keepdims=True))
            p = jnp.exp((s - m_new) * score_scale)
            factor = jnp.exp((m_run - m_new) * score_scale)
            l_run = l_run * factor + jnp.sum(p, axis=-1, keepdims=True)
            acc = acc * factor + jnp.dot(
                p.astype(jnp.bfloat16), v, preferred_element_type=jnp.float32
            )
            m_run = m_new
        out = jnp.where(valid, gate * (acc / l_run), 0.0)
        o_ref[:, g * HEAD_SIZE : (g + 1) * HEAD_SIZE] = out.astype(o_ref.dtype)


def local_attention(qidx, kidx, gate, queries, kv_all):
    rows = queries.shape[0]
    keys = kv_all.shape[0]
    group_width = (QUERY_HEADS // KEY_VALUE_HEADS) * HEAD_SIZE
    return pl.pallas_call(
        attention_kernel,
        grid=(KEY_VALUE_HEADS,),
        in_specs=[
            pl.BlockSpec((rows, 1), lambda h: (0, 0)),
            pl.BlockSpec((1, keys), lambda h: (0, 0)),
            pl.BlockSpec((rows, 1), lambda h: (0, 0)),
            pl.BlockSpec((rows, group_width), lambda h: (0, h)),
            pl.BlockSpec((keys, HEAD_SIZE), lambda h: (0, h)),
            pl.BlockSpec((keys, HEAD_SIZE), lambda h: (0, h + KEY_VALUE_HEADS)),
        ],
        out_specs=pl.BlockSpec((rows, group_width), lambda h: (0, h)),
        out_shape=jax.ShapeDtypeStruct((rows, QUERY_HEADS * HEAD_SIZE), jnp.bfloat16),
        compiler_params=pltpu.CompilerParams(dimension_semantics=("arbitrary",)),
    )(qidx, kidx, gate, queries, kv_all, kv_all)


def per_device(positions, queries, keys_values, router_weight):
    devices_x = lax.axis_size("cx")
    devices_ctx = lax.axis_size("cy") * devices_x
    my_rank = lax.axis_index("cy") * devices_x + lax.axis_index("cx")
    pair_slots = (CAP + devices_ctx - 1) // devices_ctx + 1
    offsets = shard_offsets(positions, devices_ctx)
    packed = pack_forward((keys_values,), offsets, my_rank, devices_ctx, pair_slots)
    moved = (lax.all_to_all(packed[0], ("cy", "cx"), split_axis=0, concat_axis=0, tiled=True),)
    (kv_bal,) = unpack_forward(moved, offsets, my_rank, devices_ctx, pair_slots)
    my_x = lax.axis_index("cx")
    devices_y = devices_ctx // devices_x
    my_y = lax.axis_index("cy")
    slots = kv_bal.shape[0]
    slot_half = slots // 2
    x_fwd = [(i, (i + 1) % devices_x) for i in range(devices_x)]
    x_bwd = [(i, (i - 1) % devices_x) for i in range(devices_x)]
    from_left = lax.ppermute(kv_bal, "cx", x_fwd)
    from_right = lax.ppermute(kv_bal, "cx", x_bwd)
    far_a = lax.ppermute(from_left[:slot_half], "cx", x_fwd)
    far_b = lax.ppermute(from_right[slot_half:], "cx", x_bwd)
    kv_row = jnp.concatenate([kv_bal, from_left, from_right, far_a, far_b], axis=0)
    x_blocks = [
        (my_x, 0, slots),
        ((my_x - 1) % devices_x, 0, slots),
        ((my_x + 1) % devices_x, 0, slots),
        ((my_x + 2) % devices_x, 0, slot_half),
        ((my_x + 2) % devices_x, slot_half, slots - slot_half),
    ]

    def row_key_index(y_row):
        return jnp.concatenate(
            [
                (lo + jnp.arange(n, dtype=jnp.int32)) * devices_ctx + y_row * devices_x + x
                for x, lo, n in x_blocks
            ]
        )

    group_rows = kv_row.shape[0]
    half = group_rows // 2
    fwd = [(i, (i + 1) % devices_y) for i in range(devices_y)]
    bwd = [(i, (i - 1) % devices_y) for i in range(devices_y)]
    parts = [kv_row]
    keys = [row_key_index(my_y)]
    ahead = kv_row
    behind = kv_row
    steps = devices_y // 2
    for step in range(1, steps):
        ahead = lax.ppermute(ahead, "cy", fwd)
        behind = lax.ppermute(behind, "cy", bwd)
        parts += [ahead, behind]
        keys += [row_key_index((my_y - step) % devices_y), row_key_index((my_y + step) % devices_y)]
    parts.append(lax.ppermute(ahead[:half], "cy", fwd))
    parts.append(lax.ppermute(behind[half:], "cy", bwd))
    far_keys = row_key_index((my_y + steps) % devices_y)
    keys += [far_keys[:half], far_keys[half:]]
    kv_all = jnp.concatenate(parts, axis=0)
    kidx = jnp.concatenate(keys)[None, :]
    my_start = offsets[my_rank]
    my_count = offsets[my_rank + 1] - my_start
    slot_ids = jnp.arange(CAP, dtype=jnp.int32)
    qidx = jnp.where(slot_ids < my_count, my_start + slot_ids, -1)[:, None]
    gate = router_weight.astype(jnp.float32)[:, None]
    return local_attention(qidx, kidx, gate, queries, kv_all)


def solution(mesh):
    devices = mesh.devices
    split = jax.sharding.Mesh(
        devices.reshape(devices.shape[0], devices.shape[1] // CTX_X, CTX_X), ("dp", "cy", "cx")
    )
    rows = ("dp", "cy", "cx")
    in_specs = (P("dp"), P(rows, None), P(rows, None), P(rows))
    out_specs = P(rows, None)
    return jax.shard_map(
        per_device, mesh=split, in_specs=in_specs, out_specs=out_specs, check_vma=False
    )
```
